256 devices in a mesh: row: 8 (over z_hi, y), col: 32 (over x, z_lo, core).
Axes of the slice: x: 4, y: 4, z: 8 (z_hi: 2, z_lo: 4; z = z_hi * 4 + z_lo), core: 2. Of those that a mesh axis runs over, the one named last changes fastest.
Arguments:
- features: bfloat16 [65536, 256], P(('row', 'col')), may hold values from -6 to 6
- weight: bfloat16 [256, 256], replicated, may hold values from -0.375 to 0.375
- cotangent: bfloat16 [65536, 256], P(('row', 'col')), may hold values from -6 to 6
- tile_values: bfloat16 [8, 8192, 128, 128], P('row', 'col'), may hold values from -0.0625 to 0.0625
- tile_rows: int32 [8, 8192], P('row', 'col'), may hold values from 0 to 63, as said below
- tile_cols: int32 [8, 8192], P('row', 'col'), may hold values from 0 to 15
- tile_count: int32 [8, 32], P('row', 'col'), may hold values from 32 to 256
Outputs:
- output: bfloat16 [65536, 256], P(('row', 'col'))
- feature_grad: bfloat16 [65536, 256], P(('row', 'col'))
- weight_grad: float32 [256, 256], replicated
The draws below stay inside these ranges and needn't reach their ends.
Inputs may be any that keep to these rules, and one draw needn't show every extreme that they name: Within one grid block's 256 entries the pairs (tile_rows, tile_cols) are distinct; only the first tile_count entries are occupied tiles.
All inputs are finite; a program needn't handle non-finite values.
Results may differ from the reference program's by a relative error of at most 0.006.
Values may be sent and summed in bfloat16 or wider, within the bound.
No kernel may reach another device: no remote copies, remote signals or barrier semaphores. Data moves between devices by JAX's collectives and lax.ppermute only.
A program may use at most 128 MiB of HBM per device.

```python
import jax
import jax.numpy as jnp
from jax import lax

NB = 256
F = 256
TILE = 128
KT = 256
NODES = 65536
N_ROW = 8
N_COL = 32


def slot_order(key):
    slot_total = N_COL * NB // TILE * (N_ROW * NB // TILE)
    block_keys = jax.random.split(jax.random.fold_in(key, 11), N_ROW * N_COL)

    def one_block(block_key):
        ranks = jax.random.permutation(block_key, slot_total).astype(jnp.int32) + 2
        slot_ids = lax.iota(jnp.int32, slot_total)
        ranks = jnp.where(slot_ids == slot_total - 1, 0, jnp.where(slot_ids == 0, 1, ranks))
        return jnp.argsort(ranks, stable=True)[:KT].astype(jnp.int32)
    return jax.vmap(one_block)(block_keys).reshape(N_ROW, N_COL * KT)


def draw_tile_rows(key, part):
    return (slot_order(key) // (N_ROW * NB // TILE)).astype(jnp.int32)


def draw_tile_cols(key, part):
    return (slot_order(key) % (N_ROW * NB // TILE)).astype(jnp.int32)


def draw_tile_count(key, part):
    blocks = N_ROW * N_COL
    key_one, key_two, key_three, key_four = jax.random.split(jax.random.fold_in(key, 23), 4)
    lowest = KT // 8
    first_draw = jax.random.randint(key_one, (blocks,), lowest, KT + 1, dtype=jnp.int32)
    second_draw = jax.random.randint(key_two, (blocks,), lowest, KT + 1, dtype=jnp.int32)
    counts = jnp.minimum(first_draw, second_draw)
    busiest = jax.random.randint(key_three, (), 0, blocks, dtype=jnp.int32)
    lightest = (busiest + 1 + jax.random.randint(key_four, (), 0, blocks - 1, dtype=jnp.int32)) % blocks
    block_ids = lax.iota(jnp.int32, blocks)
    counts = jnp.where(block_ids == busiest, KT, jnp.where(block_ids == lightest, lowest, counts))
    return counts.reshape(N_ROW, N_COL).astype(jnp.int32)


def block_levels(rng, shape, cuts, smallest, high):
    def one(position, shards_of):
        steps = jax.random.uniform(jax.random.fold_in(jax.random.fold_in(rng, 6), position), (shards_of,), jnp.float32, smallest / len(cuts), high / len(cuts))
        return jnp.repeat(jnp.exp(steps), shape[position] // shards_of).reshape((-1,) + (1,) * (len(shape) - position - 1))

    level = one(*cuts[0])
    for cut in cuts[1:]:
        level = level * one(*cut)
    return level


def noise(stream_key, extent, deviation, limit, cuts=(), kind=jnp.bfloat16):
    array = deviation * jax.random.normal(stream_key, extent, jnp.float32)
    if cuts:
        array = array * block_levels(stream_key, extent, cuts, -0.22, 0.18)
    return jnp.clip(array, -limit, limit).astype(kind)


def setup_inputs(seed: int = 0) -> dict:
    key_list = jax.random.split(jax.random.key(seed), 8)
    return {
        "features": noise(key_list[0], (NODES, F), 1.0, 6.0, ((0, 256),)),
        "weight": noise(key_list[1], (F, F), F ** -0.5, 0.375),
        "cotangent": noise(key_list[2], (NODES, F), 1.0, 6.0, ((0, 256),)),
        "tile_values": noise(key_list[3], (N_ROW, N_COL * KT, TILE, TILE), (N_ROW * N_COL * NB // 8) ** -0.5, 0.0625, ((0, 8), (1, 32))),
        "tile_rows": draw_tile_rows(jax.random.fold_in(key_list[7], 71), 0),
        "tile_cols": draw_tile_cols(jax.random.fold_in(key_list[7], 71), 0),
        "tile_count": draw_tile_count(jax.random.fold_in(key_list[7], 71), 0),
    }


def group_for(total):
    for candidate in (64, 32, 16, 8):
        if total % candidate == 0:
            return candidate
    return 1


def apply_tiles(tile_block, row_ids, col_ids, occupied, source, out_rows, transpose):
    tile_side = tile_block.shape[1]
    feat_width = source.shape[1]
    group_size = group_for(tile_block.shape[0])
    source_tiles = source.reshape(-1, tile_side, feat_width).astype(jnp.float32)
    zero_rows = jnp.zeros((out_rows // tile_side, tile_side, feat_width), jnp.float32)

    def advance(group_index, summed_rows):
        first_tile = (group_index * group_size).astype(jnp.int32)
        weights = lax.dynamic_slice_in_dim(tile_block, first_tile, group_size, 0).astype(jnp.float32)
        row_pick = lax.dynamic_slice_in_dim(row_ids, first_tile, group_size, 0)
        col_pick = lax.dynamic_slice_in_dim(col_ids, first_tile, group_size, 0)
        in_use = (first_tile + lax.iota(jnp.int32, group_size)) < occupied
        if transpose:
            product = jnp.einsum("kab,kaf->kbf", weights, source_tiles[row_pick])
            target = col_pick
        else:
            product = jnp.einsum("kab,kbf->kaf", weights, source_tiles[col_pick])
            target = row_pick
        product = jnp.where(in_use[:, None, None], product, jnp.zeros_like(product))
        return summed_rows.at[target].add(product)

    turn_count = ((occupied + group_size - 1) // group_size).astype(jnp.int32)
    summed_rows = lax.fori_loop(jnp.int32(0), turn_count, advance, zero_rows)
    return summed_rows.reshape(out_rows, feat_width)


def block_inputs(tile_values, tile_rows, tile_cols, tile_count, block_row, block_col):
    zero_index = jnp.zeros((), jnp.int32)
    tile_block = lax.dynamic_slice(tile_values, (block_row, block_col * KT, zero_index, zero_index), (1, KT, TILE, TILE))[0]
    row_ids = lax.dynamic_slice(tile_rows, (block_row, block_col * KT), (1, KT))[0].astype(jnp.int32)
    col_ids = lax.dynamic_slice(tile_cols, (block_row, block_col * KT), (1, KT))[0].astype(jnp.int32)
    occupied = lax.dynamic_slice(tile_count, (block_row, block_col), (1, 1))[0, 0].astype(jnp.int32)
    return tile_block, row_ids, col_ids, occupied


def reference(features, weight, cotangent, tile_values, tile_rows, tile_cols, tile_count):
    projected = jnp.dot(features, weight, preferred_element_type=jnp.float32).astype(jnp.bfloat16)
    grid = projected.reshape(N_ROW, N_COL, NB, F)

    def forward_block(block, pre):
        block = jnp.asarray(block).astype(jnp.int32)
        block_row = (block // N_COL).astype(jnp.int32)
        block_col = (block % N_COL).astype(jnp.int32)
        column_source = lax.dynamic_index_in_dim(grid, block_col, 1, keepdims=False).reshape(N_ROW * NB, F)
        tile_block, row_ids, col_ids, occupied = block_inputs(tile_values, tile_rows, tile_cols, tile_count, block_row, block_col)
        partial_value = apply_tiles(tile_block, row_ids, col_ids, occupied, column_source, N_COL * NB, False)
        offset = (block_row * (N_COL * NB)).astype(jnp.int32)
        current = lax.dynamic_slice_in_dim(pre, offset, N_COL * NB, 0)
        return lax.dynamic_update_slice_in_dim(pre, current + partial_value, offset, 0)

    pre = lax.fori_loop(0, N_ROW * N_COL, forward_block, jnp.zeros((NODES, F), jnp.float32))
    output = jax.nn.silu(pre).astype(jnp.bfloat16)
    sigma = jax.nn.sigmoid(pre)
    grad_pre = (cotangent.astype(jnp.float32) * (sigma * (1.0 + pre * (1.0 - sigma)))).astype(jnp.bfloat16)
    grad_rows = grad_pre.reshape(N_ROW, N_COL * NB, F)

    def backward_block(block, aggregated):
        block = jnp.asarray(block).astype(jnp.int32)
        block_row = (block // N_COL).astype(jnp.int32)
        block_col = (block % N_COL).astype(jnp.int32)
        zero_index = jnp.zeros((), jnp.int32)
        row_source = lax.dynamic_index_in_dim(grad_rows, block_row, 0, keepdims=False)
        tile_block, row_ids, col_ids, occupied = block_inputs(tile_values, tile_rows, tile_cols, tile_count, block_row, block_col)
        partial_value = apply_tiles(tile_block, row_ids, col_ids, occupied, row_source, N_ROW * NB, True).reshape(N_ROW, 1, NB, F)
        current = lax.dynamic_slice(aggregated, (zero_index, block_col, zero_index, zero_index), (N_ROW, 1, NB, F))
        return lax.dynamic_update_slice(aggregated, current + partial_value, (zero_index, block_col, zero_index, zero_index))

    aggregated = lax.fori_loop(0, N_ROW * N_COL, backward_block, jnp.zeros((N_ROW, N_COL, NB, F), jnp.float32))
    node_grad = aggregated.reshape(NODES, F).astype(jnp.bfloat16)
    feature_grad = jnp.dot(node_grad, weight.T, preferred_element_type=jnp.float32).astype(jnp.bfloat16)
    weight_grad = jnp.dot(features.T, node_grad, preferred_element_type=jnp.float32) * (NODES ** -0.5)
    return output, feature_grad, weight_grad
```

```python
import jax
import jax.numpy as jnp
from jax import lax
from jax.experimental import pallas as pl
from jax.experimental.pallas import tpu as pltpu
from jax.sharding import PartitionSpec as P

GROUP = 16


def tile_product(tile_block, row_ids, col_ids, occupied, source, out_rows, transpose):
    tile_count, tile_side, _ = tile_block.shape
    feat_width = source.shape[1]
    src_rows = source.shape[0]
    row_limit = (src_rows if transpose else out_rows) // tile_side - 1
    col_limit = (out_rows if transpose else src_rows) // tile_side - 1
    steps = tile_count // GROUP

    def kernel(rows_ref, cols_ref, cnt_ref, tiles_ref, src_ref, out_ref):
        g = pl.program_id(0)
        cnt = cnt_ref[0]

        @pl.when(g == 0)
        def _():
            out_ref[...] = jnp.zeros_like(out_ref)

        @pl.when(g * GROUP < cnt)
        def _():
            def body(t, carry):
                k = g * GROUP + t

                @pl.when(k < cnt)
                def _():
                    r = jnp.clip(rows_ref[k], 0, row_limit)
                    c = jnp.clip(cols_ref[k], 0, col_limit)
                    a = tiles_ref[t]
                    if transpose:
                        s = src_ref[pl.ds(pl.multiple_of(r * tile_side, tile_side), tile_side), :]
                        prod = lax.dot_general(
                            a, s, (((0,), (0,)), ((), ())), preferred_element_type=jnp.float32
                        )
                        dst = c
                    else:
                        s = src_ref[pl.ds(pl.multiple_of(c * tile_side, tile_side), tile_side), :]
                        prod = jnp.dot(a, s, preferred_element_type=jnp.float32)
                        dst = r
                    sl = pl.ds(pl.multiple_of(dst * tile_side, tile_side), tile_side)
                    out_ref[sl, :] += prod

                return carry

            lax.fori_loop(0, GROUP, body, 0, unroll=True)

    def tile_map(g, rows_ref, cols_ref, cnt_ref):
        last = jnp.maximum(cnt_ref[0] - 1, 0) // GROUP
        return (jnp.minimum(g, last), 0, 0)

    grid_spec = pltpu.PrefetchScalarGridSpec(
        num_scalar_prefetch=3,
        grid=(steps,),
        in_specs=[
            pl.BlockSpec((GROUP, tile_side, tile_side), tile_map),
            pl.BlockSpec((src_rows, feat_width), lambda g, *_: (0, 0)),
        ],
        out_specs=pl.BlockSpec((out_rows, feat_width), lambda g, *_: (0, 0)),
    )
    return pl.pallas_call(
        kernel,
        grid_spec=grid_spec,
        out_shape=jax.ShapeDtypeStruct((out_rows, feat_width), jnp.float32),
        compiler_params=pltpu.CompilerParams(
            dimension_semantics=("arbitrary",), vmem_limit_bytes=48 * 1024 * 1024
        ),
    )(row_ids, col_ids, occupied.reshape(1), tile_block, source)


def silu_grad(cot_part, pre_part):
    sigma = jax.nn.sigmoid(pre_part)
    return (cot_part.astype(jnp.float32) * (sigma * (1.0 + pre_part * (1.0 - sigma)))).astype(
        jnp.bfloat16
    )


def per_device(features, weight, cotangent, tile_values, tile_rows, tile_cols, tile_count):
    node_rows = features.shape[0]
    row_devices = lax.axis_size("row")
    col_devices = lax.axis_size("col")
    tile_block = tile_values[0]
    row_ids = tile_rows[0]
    col_ids = tile_cols[0]
    occupied = tile_count[0, 0]
    projected = jnp.dot(features, weight, preferred_element_type=jnp.float32).astype(jnp.bfloat16)
    column_source = lax.all_gather(projected, "row", axis=0, tiled=True)
    partial_value = tile_product(
        tile_block, row_ids, col_ids, occupied, column_source, col_devices * node_rows, False
    )
    pre = lax.psum_scatter(partial_value, "col", scatter_dimension=0, tiled=True)
    grad_pre = silu_grad(cotangent, pre)
    row_source = lax.all_gather(grad_pre, "col", axis=0, tiled=True)
    output = jax.nn.silu(pre).astype(jnp.bfloat16)
    back_terms = tile_product(
        tile_block, row_ids, col_ids, occupied, row_source, row_devices * node_rows, True
    )
    aggregated = lax.psum_scatter(back_terms, "row", scatter_dimension=0, tiled=True)
    node_grad = aggregated.astype(jnp.bfloat16)
    feature_grad = jnp.dot(node_grad, weight.T, preferred_element_type=jnp.float32).astype(
        jnp.bfloat16
    )
    local_term = jnp.dot(features.T, node_grad, preferred_element_type=jnp.float32)
    grad_scale = float(node_rows * row_devices * col_devices) ** (-0.5)
    weight_grad = lax.psum(local_term, ("row", "col")) * grad_scale
    return (output, feature_grad, weight_grad)


def solution(mesh):
    placed = (
        P(("row", "col"), None),
        P(),
        P(("row", "col"), None),
        P("row", "col", None, None),
        P("row", "col"),
        P("row", "col"),
        P("row", "col"),
    )
    return jax.shard_map(
        per_device,
        mesh=mesh,
        in_specs=placed,
        out_specs=(P(("row", "col"), None), P(("row", "col"), None), P()),
        check_vma=False,
    )
```

```python
import jax
import jax.numpy as jnp
from jax import lax
from jax.experimental import pallas as pl
from jax.experimental.pallas import tpu as pltpu
from jax.sharding import PartitionSpec as P

GROUP = 16


def tile_product(tile_block, row_ids, col_ids, occupied, source, out_rows, transpose, out_dtype):
    tile_count, tile_side, _ = tile_block.shape
    feat_width = source.shape[1]
    src_rows = source.shape[0]
    row_limit = (src_rows if transpose else out_rows) // tile_side - 1
    col_limit = (out_rows if transpose else src_rows) // tile_side - 1
    steps = tile_count // GROUP

    def kernel(rows_ref, cols_ref, cnt_ref, tiles_ref, src_ref, out_ref, acc_ref):
        g = pl.program_id(0)
        cnt = cnt_ref[0]

        @pl.when(g == 0)
        def _():
            acc_ref[...] = jnp.zeros_like(acc_ref)

        @pl.when(g * GROUP < cnt)
        def _():
            def body(t, carry):
                k = g * GROUP + t

                @pl.when(k < cnt)
                def _():
                    r = jnp.clip(rows_ref[k], 0, row_limit)
                    c = jnp.clip(cols_ref[k], 0, col_limit)
                    a = tiles_ref[t]
                    if transpose:
                        s = src_ref[pl.ds(pl.multiple_of(r * tile_side, tile_side), tile_side), :]
                        prod = lax.dot_general(
                            a, s, (((0,), (0,)), ((), ())), preferred_element_type=jnp.float32
                        )
                        dst = c
                    else:
                        s = src_ref[pl.ds(pl.multiple_of(c * tile_side, tile_side), tile_side), :]
                        prod = jnp.dot(a, s, preferred_element_type=jnp.float32)
                        dst = r
                    sl = pl.ds(pl.multiple_of(dst * tile_side, tile_side), tile_side)
                    acc_ref[sl, :] += prod

                return carry

            lax.fori_loop(0, GROUP, body, 0, unroll=True)

        @pl.when(g == steps - 1)
        def _():
            out_ref[...] = acc_ref[...].astype(out_ref.dtype)

    def tile_map(g, rows_ref, cols_ref, cnt_ref):
        last = jnp.maximum(cnt_ref[0] - 1, 0) // GROUP
        return (jnp.minimum(g, last), 0, 0)

    grid_spec = pltpu.PrefetchScalarGridSpec(
        num_scalar_prefetch=3,
        grid=(steps,),
        in_specs=[
            pl.BlockSpec((GROUP, tile_side, tile_side), tile_map),
            pl.BlockSpec((src_rows, feat_width), lambda g, *_: (0, 0)),
        ],
        out_specs=pl.BlockSpec((out_rows, feat_width), lambda g, *_: (0, 0)),
        scratch_shapes=[pltpu.VMEM((out_rows, feat_width), jnp.float32)],
    )
    return pl.pallas_call(
        kernel,
        grid_spec=grid_spec,
        out_shape=jax.ShapeDtypeStruct((out_rows, feat_width), out_dtype),
        compiler_params=pltpu.CompilerParams(
            dimension_semantics=("arbitrary",), vmem_limit_bytes=48 * 1024 * 1024
        ),
    )(row_ids, col_ids, occupied.reshape(1), tile_block, source)


def reduce_blocks(partial_value, axis, devices):
    pieces = partial_value.reshape(devices, -1, partial_value.shape[1])
    received = lax.all_to_all(pieces, axis, 0, 0, tiled=False)
    return received.astype(jnp.float32).sum(0)


def butterfly_sum(value, axes):
    for axis in axes:
        size = lax.axis_size(axis)
        step = 1
        while step < size:
            pairs = [(i, i ^ step) for i in range(size)]
            value = value + lax.ppermute(value, axis, pairs)
            step *= 2
    return value


def silu_grad(cot_part, pre_part):
    sigma = jax.nn.sigmoid(pre_part)
    return (cot_part.astype(jnp.float32) * (sigma * (1.0 + pre_part * (1.0 - sigma)))).astype(
        jnp.bfloat16
    )


def per_device(features, weight, cotangent, tile_values, tile_rows, tile_cols, tile_count):
    node_rows = features.shape[0]
    row_devices = lax.axis_size("row")
    col_devices = lax.axis_size("col")
    tile_block = tile_values[0]
    row_ids = tile_rows[0]
    col_ids = tile_cols[0]
    occupied = tile_count[0, 0]
    projected = jnp.dot(features, weight, preferred_element_type=jnp.float32).astype(jnp.bfloat16)
    column_source = lax.all_gather(projected, "row", axis=0, tiled=True)
    partial_value = tile_product(
        tile_block, row_ids, col_ids, occupied, column_source, col_devices * node_rows, False,
        jnp.bfloat16,
    )
    pre = reduce_blocks(partial_value, "col", col_devices)
    grad_pre = silu_grad(cotangent, pre)
    row_source = lax.all_gather(grad_pre, "col", axis=0, tiled=True)
    output = jax.nn.silu(pre).astype(jnp.bfloat16)
    back_terms = tile_product(
        tile_block, row_ids, col_ids, occupied, row_source, row_devices * node_rows, True,
        jnp.bfloat16,
    )
    aggregated = reduce_blocks(back_terms, "row", row_devices)
    node_grad = aggregated.astype(jnp.bfloat16)
    feature_grad = jnp.dot(node_grad, weight.T, preferred_element_type=jnp.float32).astype(
        jnp.bfloat16
    )
    local_term = jnp.dot(features.T, node_grad, preferred_element_type=jnp.float32)
    grad_scale = float(node_rows * row_devices * col_devices) ** (-0.5)
    weight_grad = butterfly_sum(local_term, ("col", "row")) * grad_scale
    return (output, feature_grad, weight_grad)


def solution(mesh):
    placed = (
        P(("row", "col"), None),
        P(),
        P(("row", "col"), None),
        P("row", "col", None, None),
        P("row", "col"),
        P("row", "col"),
        P("row", "col"),
    )
    return jax.shard_map(
        per_device,
        mesh=mesh,
        in_specs=placed,
        out_specs=(P(("row", "col"), None), P(("row", "col"), None), P()),
        check_vma=False,
    )
```

```python
import jax
import jax.numpy as jnp
from jax import lax
from jax.experimental import pallas as pl
from jax.experimental.pallas import tpu as pltpu
from jax.sharding import PartitionSpec as P

GROUP = 64


def tile_product(tile_block, row_ids, col_ids, occupied, source, out_rows, transpose, out_dtype):
    tile_count, tile_side, _ = tile_block.shape
    feat_width = source.shape[1]
    src_rows = source.shape[0]
    row_limit = (src_rows if transpose else out_rows) // tile_side - 1
    col_limit = (out_rows if transpose else src_rows) // tile_side - 1
    steps = tile_count // GROUP

    def kernel(rows_ref, cols_ref, cnt_ref, tiles_ref, src_ref, out_ref, acc_ref):
        g = pl.program_id(0)
        cnt = cnt_ref[0]

        @pl.when(g == 0)
        def _():
            acc_ref[...] = jnp.zeros_like(acc_ref)

        @pl.when(g * GROUP < cnt)
        def _():
            for t in range(GROUP):
                k = g * GROUP + t
                r = jnp.clip(rows_ref[k], 0, row_limit)
                c = jnp.clip(cols_ref[k], 0, col_limit)
                a = tiles_ref[t]
                if transpose:
                    s = src_ref[pl.ds(pl.multiple_of(r * tile_side, tile_side), tile_side), :]
                    prod = lax.dot_general(
                        a, s, (((0,), (0,)), ((), ())), preferred_element_type=jnp.float32
                    )
                    dst = c
                else:
                    s = src_ref[pl.ds(pl.multiple_of(c * tile_side, tile_side), tile_side), :]
                    prod = jnp.dot(a, s, preferred_element_type=jnp.float32)
                    dst = r
                prod = jnp.where(k < cnt, prod, 0.0)
                sl = pl.ds(pl.multiple_of(dst * tile_side, tile_side), tile_side)
                acc_ref[sl, :] += prod

        @pl.when(g == steps - 1)
        def _():
            out_ref[...] = acc_ref[...].astype(out_ref.dtype)

    def tile_map(g, rows_ref, cols_ref, cnt_ref):
        last = jnp.maximum(cnt_ref[0] - 1, 0) // GROUP
        return (jnp.minimum(g, last), 0, 0)

    grid_spec = pltpu.PrefetchScalarGridSpec(
        num_scalar_prefetch=3,
        grid=(steps,),
        in_specs=[
            pl.BlockSpec((GROUP, tile_side, tile_side), tile_map),
            pl.BlockSpec((src_rows, feat_width), lambda g, *_: (0, 0)),
        ],
        out_specs=pl.BlockSpec((out_rows, feat_width), lambda g, *_: (0, 0)),
        scratch_shapes=[pltpu.VMEM((out_rows, feat_width), jnp.float32)],
    )
    return pl.pallas_call(
        kernel,
        grid_spec=grid_spec,
        out_shape=jax.ShapeDtypeStruct((out_rows, feat_width), out_dtype),
        compiler_params=pltpu.CompilerParams(
            dimension_semantics=("arbitrary",), vmem_limit_bytes=48 * 1024 * 1024
        ),
    )(row_ids, col_ids, occupied.reshape(1), tile_block, source)


def reduce_blocks(partial_value, axis, devices):
    pieces = partial_value.reshape(devices, -1, partial_value.shape[1])
    received = lax.all_to_all(pieces, axis, 0, 0, tiled=False)
    return received.astype(jnp.float32).sum(0)


def butterfly_sum(value, axes):
    for axis in axes:
        size = lax.axis_size(axis)
        step = 1
        while step < size:
            pairs = [(i, i ^ step) for i in range(size)]
            value = value + lax.ppermute(value, axis, pairs)
            step *= 2
    return value


def silu_grad(cot_part, pre_part):
    sigma = jax.nn.sigmoid(pre_part)
    return (cot_part.astype(jnp.float32) * (sigma * (1.0 + pre_part * (1.0 - sigma)))).astype(
        jnp.bfloat16
    )


def per_device(features, weight, cotangent, tile_values, tile_rows, tile_cols, tile_count):
    node_rows = features.shape[0]
    row_devices = lax.axis_size("row")
    col_devices = lax.axis_size("col")
    tile_block = tile_values[0]
    row_ids = tile_rows[0]
    col_ids = tile_cols[0]
    occupied = tile_count[0, 0]
    projected = jnp.dot(features, weight, preferred_element_type=jnp.float32).astype(jnp.bfloat16)
    column_source = lax.all_gather(projected, "row", axis=0, tiled=True)
    partial_value = tile_product(
        tile_block, row_ids, col_ids, occupied, column_source, col_devices * node_rows, False,
        jnp.bfloat16,
    )
    pre = reduce_blocks(partial_value, "col", col_devices)
    grad_pre = silu_grad(cotangent, pre)
    row_source = lax.all_gather(grad_pre, "col", axis=0, tiled=True)
    output = jax.nn.silu(pre).astype(jnp.bfloat16)
    back_terms = tile_product(
        tile_block, row_ids, col_ids, occupied, row_source, row_devices * node_rows, True,
        jnp.bfloat16,
    )
    aggregated = reduce_blocks(back_terms, "row", row_devices)
    node_grad = aggregated.astype(jnp.bfloat16)
    feature_grad = jnp.dot(node_grad, weight.T, preferred_element_type=jnp.float32).astype(
        jnp.bfloat16
    )
    local_term = jnp.dot(features.T, node_grad, preferred_element_type=jnp.float32)
    grad_scale = float(node_rows * row_devices * col_devices) ** (-0.5)
    weight_grad = butterfly_sum(local_term, ("col", "row")) * grad_scale
    return (output, feature_grad, weight_grad)


def solution(mesh):
    placed = (
        P(("row", "col"), None),
        P(),
        P(("row", "col"), None),
        P("row", "col", None, None),
        P("row", "col"),
        P("row", "col"),
        P("row", "col"),
    )
    return jax.shard_map(
        per_device,
        mesh=mesh,
        in_specs=placed,
        out_specs=(P(("row", "col"), None), P(("row", "col"), None), P()),
        check_vma=False,
    )
```

```python
import jax
import jax.numpy as jnp
from jax import lax
from jax.experimental import pallas as pl
from jax.experimental.pallas import tpu as pltpu
from jax.sharding import PartitionSpec as P

GROUP = 64


def tile_product(tile_block, row_ids, col_ids, occupied, source, out_rows, transpose, out_dtype):
    tile_count, tile_side, _ = tile_block.shape
    feat_width = source.shape[1]
    src_rows = source.shape[0]
    row_limit = (src_rows if transpose else out_rows) // tile_side - 1
    col_limit = (out_rows if transpose else src_rows) // tile_side - 1
    steps = tile_count // GROUP

    def kernel(rows_ref, cols_ref, cnt_ref, tiles_ref, src_ref, out_ref, acc_ref):
        g = pl.program_id(0)
        cnt = cnt_ref[0]

        @pl.when(g == 0)
        def _():
            acc_ref[...] = jnp.zeros_like(acc_ref)

        @pl.when(g * GROUP < cnt)
        def _():
            for t in range(GROUP):
                k = g * GROUP + t
                r = jnp.clip(rows_ref[k], 0, row_limit)
                c = jnp.clip(cols_ref[k], 0, col_limit)
                a = tiles_ref[t]
                if transpose:
                    s = src_ref[pl.ds(pl.multiple_of(r * tile_side, tile_side), tile_side), :]
                    prod = lax.dot_general(
                        a, s, (((0,), (0,)), ((), ())), preferred_element_type=jnp.float32
                    )
                    dst = c
                else:
                    s = src_ref[pl.ds(pl.multiple_of(c * tile_side, tile_side), tile_side), :]
                    prod = jnp.dot(a, s, preferred_element_type=jnp.float32)
                    dst = r
                prod = jnp.where(k < cnt, prod, 0.0)
                sl = pl.ds(pl.multiple_of(dst * tile_side, tile_side), tile_side)
                acc_ref[sl, :] += prod

        @pl.when(g == steps - 1)
        def _():
            out_ref[...] = acc_ref[...].astype(out_ref.dtype)

    def tile_map(g, rows_ref, cols_ref, cnt_ref):
        last = jnp.maximum(cnt_ref[0] - 1, 0) // GROUP
        return (jnp.minimum(g, last), 0, 0)

    grid_spec = pltpu.PrefetchScalarGridSpec(
        num_scalar_prefetch=3,
        grid=(steps,),
        in_specs=[
            pl.BlockSpec((GROUP, tile_side, tile_side), tile_map),
            pl.BlockSpec((src_rows, feat_width), lambda g, *_: (0, 0)),
        ],
        out_specs=pl.BlockSpec((out_rows, feat_width), lambda g, *_: (0, 0)),
        scratch_shapes=[pltpu.VMEM((out_rows, feat_width), jnp.float32)],
    )
    return pl.pallas_call(
        kernel,
        grid_spec=grid_spec,
        out_shape=jax.ShapeDtypeStruct((out_rows, feat_width), out_dtype),
        compiler_params=pltpu.CompilerParams(
            dimension_semantics=("arbitrary",), vmem_limit_bytes=48 * 1024 * 1024
        ),
    )(row_ids, col_ids, occupied.reshape(1), tile_block, source)


def reduce_blocks(partial_value, axis, devices):
    pieces = partial_value.reshape(devices, -1, partial_value.shape[1])
    received = lax.all_to_all(pieces, axis, 0, 0, tiled=False)
    return received.astype(jnp.float32).sum(0)


def butterfly_sum(value, axes):
    for axis in axes:
        size = lax.axis_size(axis)
        step = 1
        while step < size:
            pairs = [(i, i ^ step) for i in range(size)]
            value = value + lax.ppermute(value, axis, pairs)
            step *= 2
    return value


def gather_pairs(value, axis):
    size = lax.axis_size(axis)
    me = lax.axis_index(axis)
    step = 1
    while step < size:
        other = lax.ppermute(value, axis, [(i, i ^ step) for i in range(size)])
        first = (me // step) % 2 == 0
        value = jnp.concatenate(
            [jnp.where(first, value, other), jnp.where(first, other, value)], axis=0
        )
        step *= 2
    return value


def silu_grad(cot_part, pre_part):
    sigma = jax.nn.sigmoid(pre_part)
    return (cot_part.astype(jnp.float32) * (sigma * (1.0 + pre_part * (1.0 - sigma)))).astype(
        jnp.bfloat16
    )


def per_device(features, weight, cotangent, tile_values, tile_rows, tile_cols, tile_count):
    node_rows = features.shape[0]
    row_devices = lax.axis_size("row")
    col_devices = lax.axis_size("col")
    tile_block = tile_values[0]
    row_ids = tile_rows[0]
    col_ids = tile_cols[0]
    occupied = tile_count[0, 0]
    column_source = gather_pairs(features, "row")
    partial_value = tile_product(
        tile_block, row_ids, col_ids, occupied, column_source, col_devices * node_rows, False,
        jnp.bfloat16,
    )
    mixed = reduce_blocks(partial_value, "col", col_devices)
    pre = jnp.dot(
        mixed, weight.astype(jnp.float32), precision=lax.Precision.HIGHEST,
        preferred_element_type=jnp.float32,
    )
    grad_pre = silu_grad(cotangent, pre)
    local_term = lax.dot_general(
        mixed, grad_pre.astype(jnp.float32), (((0,), (0,)), ((), ())),
        precision=lax.Precision.HIGHEST, preferred_element_type=jnp.float32,
    )
    grad_scale = float(node_rows * row_devices * col_devices) ** (-0.5)
    weight_grad = butterfly_sum(local_term, ("col", "row")) * grad_scale
    row_source = lax.all_gather(grad_pre, "col", axis=0, tiled=True)
    output = jax.nn.silu(pre).astype(jnp.bfloat16)
    back_terms = tile_product(
        tile_block, row_ids, col_ids, occupied, row_source, row_devices * node_rows, True,
        jnp.bfloat16,
    )
    aggregated = reduce_blocks(back_terms, "row", row_devices)
    node_grad = aggregated.astype(jnp.bfloat16)
    feature_grad = jnp.dot(node_grad, weight.T, preferred_element_type=jnp.float32).astype(
        jnp.bfloat16
    )
    return (output, feature_grad, weight_grad)


def solution(mesh):
    placed = (
        P(("row", "col"), None),
        P(),
        P(("row", "col"), None),
        P("row", "col", None, None),
        P("row", "col"),
        P("row", "col"),
        P("row", "col"),
    )
    return jax.shard_map(
        per_device,
        mesh=mesh,
        in_specs=placed,
        out_specs=(P(("row", "col"), None), P(("row", "col"), None), P()),
        check_vma=False,
    )
```

```python
import jax
import jax.numpy as jnp
from jax import lax
from jax.experimental import pallas as pl
from jax.experimental.pallas import tpu as pltpu
from jax.sharding import PartitionSpec as P

GROUP = 64


def tile_product(tile_block, row_ids, col_ids, occupied, source, out_rows, transpose, out_dtype):
    tile_count, tile_side, _ = tile_block.shape
    feat_width = source.shape[1]
    src_rows = source.shape[0]
    row_limit = (src_rows if transpose else out_rows) // tile_side - 1
    col_limit = (out_rows if transpose else src_rows) // tile_side - 1
    steps = tile_count // GROUP

    def kernel(rows_ref, cols_ref, cnt_ref, tiles_ref, src_ref, out_ref, acc_ref):
        g = pl.program_id(0)
        cnt = cnt_ref[0]

        @pl.when(g == 0)
        def _():
            acc_ref[...] = jnp.zeros_like(acc_ref)

        @pl.when(g * GROUP < cnt)
        def _():
            for t in range(GROUP):
                k = g * GROUP + t
                r = jnp.clip(rows_ref[k], 0, row_limit)
                c = jnp.clip(cols_ref[k], 0, col_limit)
                a = tiles_ref[t]
                if transpose:
                    s = src_ref[pl.ds(pl.multiple_of(r * tile_side, tile_side), tile_side), :]
                    prod = lax.dot_general(
                        a, s, (((0,), (0,)), ((), ())), preferred_element_type=jnp.float32
                    )
                    dst = c
                else:
                    s = src_ref[pl.ds(pl.multiple_of(c * tile_side, tile_side), tile_side), :]
                    prod = jnp.dot(a, s, preferred_element_type=jnp.float32)
                    dst = r
                prod = jnp.where(k < cnt, prod, 0.0)
                sl = pl.ds(pl.multiple_of(dst * tile_side, tile_side), tile_side)
                acc_ref[sl, :] += prod

        @pl.when(g == steps - 1)
        def _():
            out_ref[...] = acc_ref[...].astype(out_ref.dtype)

    def tile_map(g, rows_ref, cols_ref, cnt_ref):
        last = jnp.maximum(cnt_ref[0] - 1, 0) // GROUP
        return (jnp.minimum(g, last), 0, 0)

    grid_spec = pltpu.PrefetchScalarGridSpec(
        num_scalar_prefetch=3,
        grid=(steps,),
        in_specs=[
            pl.BlockSpec((GROUP, tile_side, tile_side), tile_map),
            pl.BlockSpec((src_rows, feat_width), lambda g, *_: (0, 0)),
        ],
        out_specs=pl.BlockSpec((out_rows, feat_width), lambda g, *_: (0, 0)),
        scratch_shapes=[pltpu.VMEM((out_rows, feat_width), jnp.float32)],
    )
    return pl.pallas_call(
        kernel,
        grid_spec=grid_spec,
        out_shape=jax.ShapeDtypeStruct((out_rows, feat_width), out_dtype),
        compiler_params=pltpu.CompilerParams(
            dimension_semantics=("arbitrary",), vmem_limit_bytes=48 * 1024 * 1024
        ),
    )(row_ids, col_ids, occupied.reshape(1), tile_block, source)


def reduce_blocks(partial_value, axis, devices):
    pieces = partial_value.reshape(devices, -1, partial_value.shape[1])
    received = lax.all_to_all(pieces, axis, 0, 0, tiled=False)
    return received.astype(jnp.float32).sum(0)


def butterfly_sum(value, axes):
    for axis in axes:
        size = lax.axis_size(axis)
        step = 1
        while step < size:
            pairs = [(i, i ^ step) for i in range(size)]
            value = value + lax.ppermute(value, axis, pairs)
            step *= 2
    return value


def gather_pairs(value, axis):
    size = lax.axis_size(axis)
    me = lax.axis_index(axis)
    step = 1
    while step < size:
        other = lax.ppermute(value, axis, [(i, i ^ step) for i in range(size)])
        first = (me // step) % 2 == 0
        value = jnp.concatenate(
            [jnp.where(first, value, other), jnp.where(first, other, value)], axis=0
        )
        step *= 2
    return value


def silu_grad(cot_part, pre_part):
    sigma = jax.nn.sigmoid(pre_part)
    return (cot_part.astype(jnp.float32) * (sigma * (1.0 + pre_part * (1.0 - sigma)))).astype(
        jnp.bfloat16
    )


def per_device(features, weight, cotangent, tile_values, tile_rows, tile_cols, tile_count):
    node_rows = features.shape[0]
    row_devices = lax.axis_size("row")
    col_devices = lax.axis_size("col")
    tile_block = tile_values[0]
    row_ids = tile_rows[0]
    col_ids = tile_cols[0]
    occupied = tile_count[0, 0]
    column_source = gather_pairs(features, "row")
    partial_value = tile_product(
        tile_block, row_ids, col_ids, occupied, column_source, col_devices * node_rows, False,
        jnp.bfloat16,
    )
    mixed = reduce_blocks(partial_value, "col", col_devices)
    pre = jnp.dot(
        mixed, weight.astype(jnp.float32), precision=lax.Precision.HIGHEST,
        preferred_element_type=jnp.float32,
    )
    grad_pre = silu_grad(cotangent, pre)
    local_term = lax.dot_general(
        mixed, grad_pre.astype(jnp.float32), (((0,), (0,)), ((), ())),
        precision=lax.Precision.HIGHEST, preferred_element_type=jnp.float32,
    )
    grad_scale = float(node_rows * row_devices * col_devices) ** (-0.5)
    row_summed = butterfly_sum(local_term, ("row",))
    row_source = lax.all_gather(grad_pre, "col", axis=0, tiled=True)
    row_source, row_summed = lax.optimization_barrier((row_source, row_summed))
    output = jax.nn.silu(pre).astype(jnp.bfloat16)
    back_terms = tile_product(
        tile_block, row_ids, col_ids, occupied, row_source, row_devices * node_rows, True,
        jnp.bfloat16,
    )
    weight_grad = butterfly_sum(row_summed, ("col",)) * grad_scale
    aggregated = reduce_blocks(back_terms, "row", row_devices)
    node_grad = aggregated.astype(jnp.bfloat16)
    feature_grad = jnp.dot(node_grad, weight.T, preferred_element_type=jnp.float32).astype(
        jnp.bfloat16
    )
    return (output, feature_grad, weight_grad)


def solution(mesh):
    placed = (
        P(("row", "col"), None),
        P(),
        P(("row", "col"), None),
        P("row", "col", None, None),
        P("row", "col"),
        P("row", "col"),
        P("row", "col"),
    )
    return jax.shard_map(
        per_device,
        mesh=mesh,
        in_specs=placed,
        out_specs=(P(("row", "col"), None), P(("row", "col"), None), P()),
        check_vma=False,
    )
```

```python
import jax
import jax.numpy as jnp
from jax import lax
from jax.experimental import pallas as pl
from jax.experimental.pallas import tpu as pltpu
from jax.sharding import Mesh
from jax.sharding import PartitionSpec as P

GROUP = 64


def tile_product(tile_block, row_ids, col_ids, occupied, source, out_rows, transpose, out_dtype):
    tile_count, tile_side, _ = tile_block.shape
    feat_width = source.shape[1]
    src_rows = source.shape[0]
    row_limit = (src_rows if transpose else out_rows) // tile_side - 1
    col_limit = (out_rows if transpose else src_rows) // tile_side - 1
    steps = tile_count // GROUP

    def kernel(rows_ref, cols_ref, cnt_ref, tiles_ref, src_ref, out_ref, acc_ref):
        g = pl.program_id(0)
        cnt = cnt_ref[0]

        @pl.when(g == 0)
        def _():
            acc_ref[...] = jnp.zeros_like(acc_ref)

        @pl.when(g * GROUP < cnt)
        def _():
            for t in range(GROUP):
                k = g * GROUP + t
                r = jnp.clip(rows_ref[k], 0, row_limit)
                c = jnp.clip(cols_ref[k], 0, col_limit)
                a = tiles_ref[t]
                if transpose:
                    s = src_ref[pl.ds(pl.multiple_of(r * tile_side, tile_side), tile_side), :]
                    prod = lax.dot_general(
                        a, s, (((0,), (0,)), ((), ())), preferred_element_type=jnp.float32
                    )
                    dst = c
                else:
                    s = src_ref[pl.ds(pl.multiple_of(c * tile_side, tile_side), tile_side), :]
                    prod = jnp.dot(a, s, preferred_element_type=jnp.float32)
                    dst = r
                prod = jnp.where(k < cnt, prod, 0.0)
                sl = pl.ds(pl.multiple_of(dst * tile_side, tile_side), tile_side)
                acc_ref[sl, :] += prod

        @pl.when(g == steps - 1)
        def _():
            out_ref[...] = acc_ref[...].astype(out_ref.dtype)

    def tile_map(g, rows_ref, cols_ref, cnt_ref):
        last = jnp.maximum(cnt_ref[0] - 1, 0) // GROUP
        return (jnp.minimum(g, last), 0, 0)

    grid_spec = pltpu.PrefetchScalarGridSpec(
        num_scalar_prefetch=3,
        grid=(steps,),
        in_specs=[
            pl.BlockSpec((GROUP, tile_side, tile_side), tile_map),
            pl.BlockSpec((src_rows, feat_width), lambda g, *_: (0, 0)),
        ],
        out_specs=pl.BlockSpec((out_rows, feat_width), lambda g, *_: (0, 0)),
        scratch_shapes=[pltpu.VMEM((out_rows, feat_width), jnp.float32)],
    )
    return pl.pallas_call(
        kernel,
        grid_spec=grid_spec,
        out_shape=jax.ShapeDtypeStruct((out_rows, feat_width), out_dtype),
        compiler_params=pltpu.CompilerParams(
            dimension_semantics=("arbitrary",), vmem_limit_bytes=48 * 1024 * 1024
        ),
    )(row_ids, col_ids, occupied.reshape(1), tile_block, source)


def reduce_blocks(partial_value, axis, devices):
    pieces = partial_value.reshape(devices, -1, partial_value.shape[1])
    received = lax.all_to_all(pieces, axis, 0, 0, tiled=False)
    return received.astype(jnp.float32).sum(0)


def butterfly_sum(value, axes):
    for axis in axes:
        size = lax.axis_size(axis)
        step = 1
        while step < size:
            pairs = [(i, i ^ step) for i in range(size)]
            value = value + lax.ppermute(value, axis, pairs)
            step *= 2
    return value


def gather_pairs(value, axis):
    size = lax.axis_size(axis)
    me = lax.axis_index(axis)
    step = 1
    while step < size:
        other = lax.ppermute(value, axis, [(i, i ^ step) for i in range(size)])
        first = (me // step) % 2 == 0
        value = jnp.concatenate(
            [jnp.where(first, value, other), jnp.where(first, other, value)], axis=0
        )
        step *= 2
    return value


def reduce_pairs_then_blocks(partial_value, outer, inner):
    outer_size = lax.axis_size(outer)
    inner_size = lax.axis_size(inner)
    pieces = partial_value.reshape(outer_size, inner_size, -1, partial_value.shape[1])
    me = lax.axis_index(inner)
    keep = jnp.take(pieces, me, axis=1)
    send = jnp.take(pieces, inner_size - 1 - me, axis=1)
    paired = keep + lax.ppermute(send, inner, [(i, inner_size - 1 - i) for i in range(inner_size)])
    received = lax.all_to_all(paired.astype(jnp.bfloat16), outer, 0, 0, tiled=False)
    return received.astype(jnp.float32).sum(0)


def silu_grad(cot_part, pre_part):
    sigma = jax.nn.sigmoid(pre_part)
    return (cot_part.astype(jnp.float32) * (sigma * (1.0 + pre_part * (1.0 - sigma)))).astype(
        jnp.bfloat16
    )


def per_device(features, weight, cotangent, tile_values, tile_rows, tile_cols, tile_count):
    node_rows = features.shape[0]
    row_devices = lax.axis_size("row")
    col_axes = ("colhi", "core")
    col_devices = lax.axis_size(col_axes)
    tile_block = tile_values[0]
    row_ids = tile_rows[0]
    col_ids = tile_cols[0]
    occupied = tile_count[0, 0]
    column_source = gather_pairs(features, "row")
    partial_value = tile_product(
        tile_block, row_ids, col_ids, occupied, column_source, col_devices * node_rows, False,
        jnp.float32,
    )
    mixed = reduce_pairs_then_blocks(partial_value, "colhi", "core")
    pre = jnp.dot(
        mixed, weight.astype(jnp.float32), precision=lax.Precision.HIGHEST,
        preferred_element_type=jnp.float32,
    )
    grad_pre = silu_grad(cotangent, pre)
    local_term = lax.dot_general(
        mixed, grad_pre.astype(jnp.float32), (((0,), (0,)), ((), ())),
        precision=lax.Precision.HIGHEST, preferred_element_type=jnp.float32,
    )
    grad_scale = float(node_rows * row_devices * col_devices) ** (-0.5)
    row_summed = butterfly_sum(local_term, ("row",))
    row_source = lax.all_gather(grad_pre, col_axes, axis=0, tiled=True)
    row_source, row_summed = lax.optimization_barrier((row_source, row_summed))
    output = jax.nn.silu(pre).astype(jnp.bfloat16)
    back_terms = tile_product(
        tile_block, row_ids, col_ids, occupied, row_source, row_devices * node_rows, True,
        jnp.bfloat16,
    )
    weight_grad = butterfly_sum(row_summed, ("core", "colhi")) * grad_scale
    aggregated = reduce_blocks(back_terms, "row", row_devices)
    node_grad = aggregated.astype(jnp.bfloat16)
    feature_grad = jnp.dot(node_grad, weight.T, preferred_element_type=jnp.float32).astype(
        jnp.bfloat16
    )
    return (output, feature_grad, weight_grad)


def solution(mesh):
    cores = 2
    devices = mesh.devices.reshape(mesh.shape["row"], mesh.shape["col"] // cores, cores)
    split_mesh = Mesh(devices, ("row", "colhi", "core"))
    nodes = ("row", "colhi", "core")
    blocks = ("colhi", "core")
    placed = (
        P(nodes, None),
        P(),
        P(nodes, None),
        P("row", blocks, None, None),
        P("row", blocks),
        P("row", blocks),
        P("row", blocks),
    )
    return jax.shard_map(
        per_device,
        mesh=split_mesh,
        in_specs=placed,
        out_specs=(P(nodes, None), P(nodes, None), P()),
        check_vma=False,
    )
```

```python
import jax
import jax.numpy as jnp
from jax import lax
from jax.experimental import pallas as pl
from jax.experimental.pallas import tpu as pltpu
from jax.sharding import Mesh
from jax.sharding import PartitionSpec as P

GROUP = 64


def tile_product(tile_block, row_ids, col_ids, occupied, source, out_rows, transpose, out_dtype):
    tile_count, tile_side, _ = tile_block.shape
    feat_width = source.shape[1]
    src_rows = source.shape[0]
    row_limit = (src_rows if transpose else out_rows) // tile_side - 1
    col_limit = (out_rows if transpose else src_rows) // tile_side - 1
    steps = tile_count // GROUP

    def kernel(rows_ref, cols_ref, cnt_ref, tiles_ref, src_ref, out_ref, acc_ref):
        g = pl.program_id(0)
        cnt = cnt_ref[0]

        @pl.when(g == 0)
        def _():
            acc_ref[...] = jnp.zeros_like(acc_ref)

        @pl.when(g * GROUP < cnt)
        def _():
            for t in range(GROUP):
                k = g * GROUP + t
                r = jnp.clip(rows_ref[k], 0, row_limit)
                c = jnp.clip(cols_ref[k], 0, col_limit)
                a = tiles_ref[t]
                if transpose:
                    s = src_ref[pl.ds(pl.multiple_of(r * tile_side, tile_side), tile_side), :]
                    prod = lax.dot_general(
                        a, s, (((0,), (0,)), ((), ())), preferred_element_type=jnp.float32
                    )
                    dst = c
                else:
                    s = src_ref[pl.ds(pl.multiple_of(c * tile_side, tile_side), tile_side), :]
                    prod = jnp.dot(a, s, preferred_element_type=jnp.float32)
                    dst = r
                prod = jnp.where(k < cnt, prod, 0.0)
                sl = pl.ds(pl.multiple_of(dst * tile_side, tile_side), tile_side)
                acc_ref[sl, :] += prod

        @pl.when(g == steps - 1)
        def _():
            out_ref[...] = acc_ref[...].astype(out_ref.dtype)

    def tile_map(g, rows_ref, cols_ref, cnt_ref):
        last = jnp.maximum(cnt_ref[0] - 1, 0) // GROUP
        return (jnp.minimum(g, last), 0, 0)

    grid_spec = pltpu.PrefetchScalarGridSpec(
        num_scalar_prefetch=3,
        grid=(steps,),
        in_specs=[
            pl.BlockSpec((GROUP, tile_side, tile_side), tile_map),
            pl.BlockSpec((src_rows, feat_width), lambda g, *_: (0, 0)),
        ],
        out_specs=pl.BlockSpec((out_rows, feat_width), lambda g, *_: (0, 0)),
        scratch_shapes=[pltpu.VMEM((out_rows, feat_width), jnp.float32)],
    )
    return pl.pallas_call(
        kernel,
        grid_spec=grid_spec,
        out_shape=jax.ShapeDtypeStruct((out_rows, feat_width), out_dtype),
        compiler_params=pltpu.CompilerParams(
            dimension_semantics=("arbitrary",), vmem_limit_bytes=48 * 1024 * 1024
        ),
    )(row_ids, col_ids, occupied.reshape(1), tile_block, source)


def reduce_blocks(partial_value, axis, devices):
    pieces = partial_value.reshape(devices, -1, partial_value.shape[1])
    received = lax.all_to_all(pieces, axis, 0, 0, tiled=False)
    return received.astype(jnp.float32).sum(0)


def butterfly_sum(value, axes):
    for axis in axes:
        size = lax.axis_size(axis)
        step = 1
        while step < size:
            pairs = [(i, i ^ step) for i in range(size)]
            value = value + lax.ppermute(value, axis, pairs)
            step *= 2
    return value


def gather_pairs(value, axis):
    size = lax.axis_size(axis)
    me = lax.axis_index(axis)
    step = 1
    while step < size:
        other = lax.ppermute(value, axis, [(i, i ^ step) for i in range(size)])
        first = (me // step) % 2 == 0
        value = jnp.concatenate(
            [jnp.where(first, value, other), jnp.where(first, other, value)], axis=0
        )
        step *= 2
    return value


def reduce_pairs_then_blocks(partial_value, outer, inner):
    outer_size = lax.axis_size(outer)
    inner_size = lax.axis_size(inner)
    pieces = partial_value.reshape(outer_size, inner_size, -1, partial_value.shape[1])
    me = lax.axis_index(inner)
    keep = jnp.take(pieces, me, axis=1)
    send = jnp.take(pieces, inner_size - 1 - me, axis=1)
    paired = keep + lax.ppermute(send, inner, [(i, inner_size - 1 - i) for i in range(inner_size)])
    received = lax.all_to_all(paired.astype(jnp.bfloat16), outer, 0, 0, tiled=False)
    return received.astype(jnp.float32).sum(0)


def silu_grad(cot_part, pre_part):
    sigma = jax.nn.sigmoid(pre_part)
    return (cot_part.astype(jnp.float32) * (sigma * (1.0 + pre_part * (1.0 - sigma)))).astype(
        jnp.bfloat16
    )


def per_device(features, weight, cotangent, tile_values, tile_rows, tile_cols, tile_count):
    node_rows = features.shape[0]
    row_devices = lax.axis_size("row")
    col_axes = ("colhi", "core")
    col_devices = lax.axis_size(col_axes)
    tile_block = tile_values[0]
    row_ids = tile_rows[0]
    col_ids = tile_cols[0]
    occupied = tile_count[0, 0]
    column_source = gather_pairs(features, "row")
    partial_value = tile_product(
        tile_block, row_ids, col_ids, occupied, column_source, col_devices * node_rows, False,
        jnp.float32,
    )
    mixed = reduce_pairs_then_blocks(partial_value, "colhi", "core")
    pre = jnp.dot(
        mixed, weight.astype(jnp.float32), precision=lax.Precision.HIGHEST,
        preferred_element_type=jnp.float32,
    )
    grad_pre = silu_grad(cotangent, pre)
    local_term = lax.dot_general(
        mixed, grad_pre.astype(jnp.float32), (((0,), (0,)), ((), ())),
        precision=lax.Precision.HIGHEST, preferred_element_type=jnp.float32,
    )
    grad_scale = float(node_rows * row_devices * col_devices) ** (-0.5)
    weight_grad = butterfly_sum(local_term, ("row", "core", "colhi")) * grad_scale
    row_source = lax.all_gather(grad_pre, col_axes, axis=0, tiled=True)
    row_source, weight_grad = lax.optimization_barrier((row_source, weight_grad))
    output = jax.nn.silu(pre).astype(jnp.bfloat16)
    back_terms = tile_product(
        tile_block, row_ids, col_ids, occupied, row_source, row_devices * node_rows, True,
        jnp.bfloat16,
    )
    aggregated = reduce_blocks(back_terms, "row", row_devices)
    node_grad = aggregated.astype(jnp.bfloat16)
    feature_grad = jnp.dot(node_grad, weight.T, preferred_element_type=jnp.float32).astype(
        jnp.bfloat16
    )
    return (output, feature_grad, weight_grad)


def solution(mesh):
    cores = 2
    devices = mesh.devices.reshape(mesh.shape["row"], mesh.shape["col"] // cores, cores)
    split_mesh = Mesh(devices, ("row", "colhi", "core"))
    nodes = ("row", "colhi", "core")
    blocks = ("colhi", "core")
    placed = (
        P(nodes, None),
        P(),
        P(nodes, None),
        P("row", blocks, None, None),
        P("row", blocks),
        P("row", blocks),
        P("row", blocks),
    )
    return jax.shard_map(
        per_device,
        mesh=split_mesh,
        in_specs=placed,
        out_specs=(P(nodes, None), P(nodes, None), P()),
        check_vma=False,
    )
```

```python
import jax
import jax.numpy as jnp
from jax import lax
from jax.experimental import pallas as pl
from jax.experimental.pallas import tpu as pltpu
from jax.sharding import Mesh
from jax.sharding import PartitionSpec as P

GROUP = 64


def tile_product(
    tile_block, row_ids, col_ids, occupied, source, out_rows, transpose, out_dtype,
    cores=1, dev_tiles=1,
):
    tile_count, tile_side, _ = tile_block.shape
    feat_width = source.shape[1]
    src_rows = source.shape[0]
    row_limit = (src_rows if transpose else out_rows) // tile_side - 1
    col_limit = (out_rows if transpose else src_rows) // tile_side - 1
    steps = tile_count // GROUP
    out_tiles = out_rows // tile_side

    def kernel(rows_ref, cols_ref, cnt_ref, tiles_ref, src_ref, out_ref, acc_ref):
        g = pl.program_id(0)
        cnt = cnt_ref[0]

        @pl.when(g == 0)
        def _():
            acc_ref[...] = jnp.zeros_like(acc_ref)

        @pl.when(g * GROUP < cnt)
        def _():
            for t in range(GROUP):
                k = g * GROUP + t
                r = jnp.clip(rows_ref[k], 0, row_limit)
                c = jnp.clip(cols_ref[k], 0, col_limit)
                a = tiles_ref[t]
                if transpose:
                    s = src_ref[pl.ds(pl.multiple_of(r * tile_side, tile_side), tile_side), :]
                    prod = lax.dot_general(
                        a, s, (((0,), (0,)), ((), ())), preferred_element_type=jnp.float32
                    )
                    dst = c
                else:
                    s = src_ref[pl.ds(pl.multiple_of(c * tile_side, tile_side), tile_side), :]
                    prod = jnp.dot(a, s, preferred_element_type=jnp.float32)
                    dev, part = r // dev_tiles, r % dev_tiles
                    per_core = out_tiles // dev_tiles // cores
                    dst = ((dev % cores) * per_core + dev // cores) * dev_tiles + part
                prod = jnp.where(k < cnt, prod, 0.0)
                sl = pl.ds(pl.multiple_of(dst * tile_side, tile_side), tile_side)
                acc_ref[sl, :] += prod

        @pl.when(g == steps - 1)
        def _():
            out_ref[...] = acc_ref[...].astype(out_ref.dtype)

    def tile_map(g, rows_ref, cols_ref, cnt_ref):
        last = jnp.maximum(cnt_ref[0] - 1, 0) // GROUP
        return (jnp.minimum(g, last), 0, 0)

    grid_spec = pltpu.PrefetchScalarGridSpec(
        num_scalar_prefetch=3,
        grid=(steps,),
        in_specs=[
            pl.BlockSpec((GROUP, tile_side, tile_side), tile_map),
            pl.BlockSpec((src_rows, feat_width), lambda g, *_: (0, 0)),
        ],
        out_specs=pl.BlockSpec((out_rows, feat_width), lambda g, *_: (0, 0)),
        scratch_shapes=[pltpu.VMEM((out_rows, feat_width), jnp.float32)],
    )
    return pl.pallas_call(
        kernel,
        grid_spec=grid_spec,
        out_shape=jax.ShapeDtypeStruct((out_rows, feat_width), out_dtype),
        compiler_params=pltpu.CompilerParams(
            dimension_semantics=("arbitrary",), vmem_limit_bytes=48 * 1024 * 1024
        ),
    )(row_ids, col_ids, occupied.reshape(1), tile_block, source)


def reduce_blocks(partial_value, axis, devices):
    pieces = partial_value.reshape(devices, -1, partial_value.shape[1])
    received = lax.all_to_all(pieces, axis, 0, 0, tiled=False)
    return received.astype(jnp.float32).sum(0)


def butterfly_sum(value, axes):
    for axis in axes:
        size = lax.axis_size(axis)
        step = 1
        while step < size:
            pairs = [(i, i ^ step) for i in range(size)]
            value = value + lax.ppermute(value, axis, pairs)
            step *= 2
    return value


def split_sum(value, outer, inner):
    plan = []
    for axis in outer:
        step = 1
        while step < lax.axis_size(axis):
            plan.append((axis, step))
            step *= 2
    for axis, step in plan:
        size = lax.axis_size(axis)
        low = (lax.axis_index(axis) // step) % 2 == 0
        half = value.shape[0] // 2
        head, tail = value[:half], value[half:]
        send = jnp.where(low, tail, head)
        keep = jnp.where(low, head, tail)
        value = keep + lax.ppermute(send, axis, [(i, i ^ step) for i in range(size)])
    value = butterfly_sum(value, inner)
    for axis, step in reversed(plan):
        size = lax.axis_size(axis)
        low = (lax.axis_index(axis) // step) % 2 == 0
        other = lax.ppermute(value, axis, [(i, i ^ step) for i in range(size)])
        value = jnp.concatenate(
            [jnp.where(low, value, other), jnp.where(low, other, value)], axis=0
        )
    return value


def gather_pairs(value, axis):
    size = lax.axis_size(axis)
    me = lax.axis_index(axis)
    step = 1
    while step < size:
        other = lax.ppermute(value, axis, [(i, i ^ step) for i in range(size)])
        first = (me // step) % 2 == 0
        value = jnp.concatenate(
            [jnp.where(first, value, other), jnp.where(first, other, value)], axis=0
        )
        step *= 2
    return value


def reduce_pairs_then_blocks(partial_value, outer, inner):
    outer_size = lax.axis_size(outer)
    inner_size = lax.axis_size(inner)
    pieces = partial_value.reshape(inner_size, outer_size, -1, partial_value.shape[1])
    me = lax.axis_index(inner)
    keep = lax.dynamic_index_in_dim(pieces, me, 0, keepdims=False)
    send = lax.dynamic_index_in_dim(pieces, inner_size - 1 - me, 0, keepdims=False)
    paired = keep + lax.ppermute(send, inner, [(i, inner_size - 1 - i) for i in range(inner_size)])
    received = lax.all_to_all(paired.astype(jnp.bfloat16), outer, 0, 0, tiled=False)
    return received.astype(jnp.float32).sum(0)


def silu_grad(cot_part, pre_part):
    sigma = jax.nn.sigmoid(pre_part)
    return (cot_part.astype(jnp.float32) * (sigma * (1.0 + pre_part * (1.0 - sigma)))).astype(
        jnp.bfloat16
    )


def per_device(features, weight, cotangent, tile_values, tile_rows, tile_cols, tile_count):
    node_rows = features.shape[0]
    row_devices = lax.axis_size("row")
    col_axes = ("colhi", "core")
    col_devices = lax.axis_size(col_axes)
    tile_block = tile_values[0]
    row_ids = tile_rows[0]
    col_ids = tile_cols[0]
    occupied = tile_count[0, 0]
    column_source = gather_pairs(features, "row")
    partial_value = tile_product(
        tile_block, row_ids, col_ids, occupied, column_source, col_devices * node_rows, False,
        jnp.float32, cores=lax.axis_size("core"), dev_tiles=node_rows // tile_block.shape[1],
    )
    mixed = reduce_pairs_then_blocks(partial_value, "colhi", "core")
    pre = jnp.dot(
        mixed, weight.astype(jnp.float32), precision=lax.Precision.HIGHEST,
        preferred_element_type=jnp.float32,
    )
    grad_pre = silu_grad(cotangent, pre)
    local_term = lax.dot_general(
        mixed, grad_pre.astype(jnp.float32), (((0,), (0,)), ((), ())),
        precision=lax.Precision.HIGHEST, preferred_element_type=jnp.float32,
    )
    grad_scale = float(node_rows * row_devices * col_devices) ** (-0.5)
    weight_grad = split_sum(local_term, ("row",), ("core", "colhi")) * grad_scale
    row_source = lax.all_gather(grad_pre, col_axes, axis=0, tiled=True)
    row_source, weight_grad = lax.optimization_barrier((row_source, weight_grad))
    output = jax.nn.silu(pre).astype(jnp.bfloat16)
    back_terms = tile_product(
        tile_block, row_ids, col_ids, occupied, row_source, row_devices * node_rows, True,
        jnp.bfloat16,
    )
    aggregated = reduce_blocks(back_terms, "row", row_devices)
    node_grad = aggregated.astype(jnp.bfloat16)
    feature_grad = jnp.dot(node_grad, weight.T, preferred_element_type=jnp.float32).astype(
        jnp.bfloat16
    )
    return (output, feature_grad, weight_grad)


def solution(mesh):
    cores = 2
    devices = mesh.devices.reshape(mesh.shape["row"], mesh.shape["col"] // cores, cores)
    split_mesh = Mesh(devices, ("row", "colhi", "core"))
    nodes = ("row", "colhi", "core")
    blocks = ("colhi", "core")
    placed = (
        P(nodes, None),
        P(),
        P(nodes, None),
        P("row", blocks, None, None),
        P("row", blocks),
        P("row", blocks),
        P("row", blocks),
    )
    return jax.shard_map(
        per_device,
        mesh=split_mesh,
        in_specs=placed,
        out_specs=(P(nodes, None), P(nodes, None), P()),
        check_vma=False,
    )
```

```python
import jax
import jax.numpy as jnp
from jax import lax
from jax.experimental import pallas as pl
from jax.experimental.pallas import tpu as pltpu
from jax.sharding import Mesh
from jax.sharding import PartitionSpec as P

GROUP = 64


def tile_product(
    tile_block, row_ids, col_ids, occupied, source, out_rows, transpose, out_dtype,
    cores=1, dev_tiles=1, core_index=None,
):
    tile_count, tile_side, _ = tile_block.shape
    feat_width = source.shape[1]
    src_rows = source.shape[0]
    row_limit = (src_rows if transpose else out_rows) // tile_side - 1
    col_limit = (out_rows if transpose else src_rows) // tile_side - 1
    steps = tile_count // GROUP
    part_rows = out_rows // cores
    if core_index is None:
        core_index = jnp.zeros((), jnp.int32)

    def kernel(rows_ref, cols_ref, cnt_ref, me_ref, tiles_ref, src_ref, *refs):
        out_refs, acc_ref = refs[:cores], refs[cores]
        g = pl.program_id(0)
        cnt = cnt_ref[0]
        me = me_ref[0]

        @pl.when(g == 0)
        def _():
            acc_ref[...] = jnp.zeros_like(acc_ref)

        @pl.when(g * GROUP < cnt)
        def _():
            for t in range(GROUP):
                k = g * GROUP + t
                r = jnp.clip(rows_ref[k], 0, row_limit)
                c = jnp.clip(cols_ref[k], 0, col_limit)
                a = tiles_ref[t]
                if transpose:
                    s = src_ref[pl.ds(pl.multiple_of(r * tile_side, tile_side), tile_side), :]
                    prod = lax.dot_general(
                        a, s, (((0,), (0,)), ((), ())), preferred_element_type=jnp.float32
                    )
                    sel = 0
                    dst = c
                else:
                    s = src_ref[pl.ds(pl.multiple_of(c * tile_side, tile_side), tile_side), :]
                    prod = jnp.dot(a, s, preferred_element_type=jnp.float32)
                    dev, part = r // dev_tiles, r % dev_tiles
                    sel = (dev % cores - me + cores) % cores
                    dst = (dev // cores) * dev_tiles + part
                prod = jnp.where(k < cnt, prod, 0.0)
                sl = pl.ds(pl.multiple_of(dst * tile_side, tile_side), tile_side)
                acc_ref[sel, sl, :] += prod

        @pl.when(g == steps - 1)
        def _():
            for i in range(cores):
                out_refs[i][...] = acc_ref[i].astype(out_refs[i].dtype)

    def tile_map(g, rows_ref, cols_ref, cnt_ref, me_ref):
        last = jnp.maximum(cnt_ref[0] - 1, 0) // GROUP
        return (jnp.minimum(g, last), 0, 0)

    grid_spec = pltpu.PrefetchScalarGridSpec(
        num_scalar_prefetch=4,
        grid=(steps,),
        in_specs=[
            pl.BlockSpec((GROUP, tile_side, tile_side), tile_map),
            pl.BlockSpec((src_rows, feat_width), lambda g, *_: (0, 0)),
        ],
        out_specs=[
            pl.BlockSpec((part_rows, feat_width), lambda g, *_: (0, 0)) for _ in range(cores)
        ],
        scratch_shapes=[pltpu.VMEM((cores, part_rows, feat_width), jnp.float32)],
    )
    return pl.pallas_call(
        kernel,
        grid_spec=grid_spec,
        out_shape=[jax.ShapeDtypeStruct((part_rows, feat_width), out_dtype) for _ in range(cores)],
        compiler_params=pltpu.CompilerParams(
            dimension_semantics=("arbitrary",), vmem_limit_bytes=48 * 1024 * 1024
        ),
    )(row_ids, col_ids, occupied.reshape(1), core_index.reshape(1).astype(jnp.int32), tile_block, source)


def reduce_blocks(partial_value, axis, devices):
    pieces = partial_value.reshape(devices, -1, partial_value.shape[1])
    received = lax.all_to_all(pieces, axis, 0, 0, tiled=False)
    return received.astype(jnp.float32).sum(0)


def butterfly_sum(value, axes):
    for axis in axes:
        size = lax.axis_size(axis)
        step = 1
        while step < size:
            pairs = [(i, i ^ step) for i in range(size)]
            value = value + lax.ppermute(value, axis, pairs)
            step *= 2
    return value


def split_sum(value, outer, inner):
    plan = []
    for axis in outer:
        step = 1
        while step < lax.axis_size(axis):
            plan.append((axis, step))
            step *= 2
    for axis, step in plan:
        size = lax.axis_size(axis)
        low = (lax.axis_index(axis) // step) % 2 == 0
        half = value.shape[0] // 2
        head, tail = value[:half], value[half:]
        send = jnp.where(low, tail, head)
        keep = jnp.where(low, head, tail)
        value = keep + lax.ppermute(send, axis, [(i, i ^ step) for i in range(size)])
    value = butterfly_sum(value, inner)
    for axis, step in reversed(plan):
        size = lax.axis_size(axis)
        low = (lax.axis_index(axis) // step) % 2 == 0
        other = lax.ppermute(value, axis, [(i, i ^ step) for i in range(size)])
        value = jnp.concatenate(
            [jnp.where(low, value, other), jnp.where(low, other, value)], axis=0
        )
    return value


def gather_pairs(value, axis):
    size = lax.axis_size(axis)
    me = lax.axis_index(axis)
    step = 1
    while step < size:
        other = lax.ppermute(value, axis, [(i, i ^ step) for i in range(size)])
        first = (me // step) % 2 == 0
        value = jnp.concatenate(
            [jnp.where(first, value, other), jnp.where(first, other, value)], axis=0
        )
        step *= 2
    return value


def reduce_pairs_then_blocks(keep, send, outer, inner):
    outer_size = lax.axis_size(outer)
    inner_size = lax.axis_size(inner)
    keep = keep.reshape(outer_size, -1, keep.shape[1])
    send = send.reshape(outer_size, -1, send.shape[1])
    paired = keep + lax.ppermute(send, inner, [(i, inner_size - 1 - i) for i in range(inner_size)])
    received = lax.all_to_all(paired.astype(jnp.bfloat16), outer, 0, 0, tiled=False)
    return received.astype(jnp.float32).sum(0)


def silu_grad(cot_part, pre_part):
    sigma = jax.nn.sigmoid(pre_part)
    return (cot_part.astype(jnp.float32) * (sigma * (1.0 + pre_part * (1.0 - sigma)))).astype(
        jnp.bfloat16
    )


def per_device(features, weight, cotangent, tile_values, tile_rows, tile_cols, tile_count):
    node_rows = features.shape[0]
    row_devices = lax.axis_size("row")
    col_axes = ("colhi", "core")
    col_devices = lax.axis_size(col_axes)
    tile_block = tile_values[0]
    row_ids = tile_rows[0]
    col_ids = tile_cols[0]
    occupied = tile_count[0, 0]
    column_source = gather_pairs(features, "row")
    keep, send = tile_product(
        tile_block, row_ids, col_ids, occupied, column_source, col_devices * node_rows, False,
        jnp.float32, cores=lax.axis_size("core"), dev_tiles=node_rows // tile_block.shape[1],
        core_index=lax.axis_index("core"),
    )
    mixed = reduce_pairs_then_blocks(keep, send, "colhi", "core")
    pre = jnp.dot(
        mixed, weight.astype(jnp.float32), precision=lax.Precision.HIGHEST,
        preferred_element_type=jnp.float32,
    )
    grad_pre = silu_grad(cotangent, pre)
    local_term = lax.dot_general(
        mixed, grad_pre.astype(jnp.float32), (((0,), (0,)), ((), ())),
        precision=lax.Precision.HIGHEST, preferred_element_type=jnp.float32,
    )
    grad_scale = float(node_rows * row_devices * col_devices) ** (-0.5)
    weight_grad = split_sum(local_term, ("row",), ("core", "colhi")) * grad_scale
    row_source = lax.all_gather(grad_pre, col_axes, axis=0, tiled=True)
    row_source, weight_grad = lax.optimization_barrier((row_source, weight_grad))
    output = jax.nn.silu(pre).astype(jnp.bfloat16)
    (back_terms,) = tile_product(
        tile_block, row_ids, col_ids, occupied, row_source, row_devices * node_rows, True,
        jnp.bfloat16,
    )
    aggregated = reduce_blocks(back_terms, "row", row_devices)
    node_grad = aggregated.astype(jnp.bfloat16)
    feature_grad = jnp.dot(node_grad, weight.T, preferred_element_type=jnp.float32).astype(
        jnp.bfloat16
    )
    return (output, feature_grad, weight_grad)


def solution(mesh):
    cores = 2
    devices = mesh.devices.reshape(mesh.shape["row"], mesh.shape["col"] // cores, cores)
    split_mesh = Mesh(devices, ("row", "colhi", "core"))
    nodes = ("row", "colhi", "core")
    blocks = ("colhi", "core")
    placed = (
        P(nodes, None),
        P(),
        P(nodes, None),
        P("row", blocks, None, None),
        P("row", blocks),
        P("row", blocks),
        P("row", blocks),
    )
    return jax.shard_map(
        per_device,
        mesh=split_mesh,
        in_specs=placed,
        out_specs=(P(nodes, None), P(nodes, None), P()),
        check_vma=False,
    )
```

```python
import jax
import jax.numpy as jnp
from jax import lax
from jax.experimental import pallas as pl
from jax.experimental.pallas import tpu as pltpu
from jax.sharding import Mesh
from jax.sharding import PartitionSpec as P

GROUP = 64


def tile_product(
    tile_block, row_ids, col_ids, occupied, source, out_rows, transpose, out_dtype,
    cores=1, dev_tiles=1, core_index=None, src_bits=0,
):
    tile_count, tile_side, _ = tile_block.shape
    feat_width = source.shape[1]
    src_rows = source.shape[0]
    row_limit = (src_rows if transpose else out_rows) // tile_side - 1
    col_limit = (out_rows if transpose else src_rows) // tile_side - 1
    steps = tile_count // GROUP
    part_rows = out_rows // cores
    if core_index is None:
        core_index = jnp.zeros((), jnp.int32)

    def kernel(rows_ref, cols_ref, cnt_ref, me_ref, tiles_ref, src_ref, *refs):
        out_refs, acc_ref = refs[:cores], refs[cores]
        g = pl.program_id(0)
        cnt = cnt_ref[0]
        me = me_ref[0]

        @pl.when(g == 0)
        def _():
            acc_ref[...] = jnp.zeros_like(acc_ref)

        @pl.when(g * GROUP < cnt)
        def _():
            for t in range(GROUP):
                k = g * GROUP + t
                r = jnp.clip(rows_ref[k], 0, row_limit)
                c = jnp.clip(cols_ref[k], 0, col_limit)
                a = tiles_ref[t]
                if transpose:
                    s = src_ref[pl.ds(pl.multiple_of(r * tile_side, tile_side), tile_side), :]
                    prod = lax.dot_general(
                        a, s, (((0,), (0,)), ((), ())), preferred_element_type=jnp.float32
                    )
                    sel = 0
                    dst = c
                else:
                    src_dev, src_part = c // dev_tiles, c % dev_tiles
                    flipped = 0
                    for bit in range(src_bits):
                        flipped = flipped + ((src_dev // 2**bit) % 2) * 2 ** (src_bits - 1 - bit)
                    if src_bits:
                        c = flipped * dev_tiles + src_part
                    s = src_ref[pl.ds(pl.multiple_of(c * tile_side, tile_side), tile_side), :]
                    prod = jnp.dot(a, s, preferred_element_type=jnp.float32)
                    dev, part = r // dev_tiles, r % dev_tiles
                    sel = (dev % cores - me + cores) % cores
                    dst = (dev // cores) * dev_tiles + part
                prod = jnp.where(k < cnt, prod, 0.0)
                sl = pl.ds(pl.multiple_of(dst * tile_side, tile_side), tile_side)
                acc_ref[sel, sl, :] += prod

        @pl.when(g == steps - 1)
        def _():
            for i in range(cores):
                out_refs[i][...] = acc_ref[i].astype(out_refs[i].dtype)

    def tile_map(g, rows_ref, cols_ref, cnt_ref, me_ref):
        last = jnp.maximum(cnt_ref[0] - 1, 0) // GROUP
        return (jnp.minimum(g, last), 0, 0)

    grid_spec = pltpu.PrefetchScalarGridSpec(
        num_scalar_prefetch=4,
        grid=(steps,),
        in_specs=[
            pl.BlockSpec((GROUP, tile_side, tile_side), tile_map),
            pl.BlockSpec((src_rows, feat_width), lambda g, *_: (0, 0)),
        ],
        out_specs=[
            pl.BlockSpec((part_rows, feat_width), lambda g, *_: (0, 0)) for _ in range(cores)
        ],
        scratch_shapes=[pltpu.VMEM((cores, part_rows, feat_width), jnp.float32)],
    )
    return pl.pallas_call(
        kernel,
        grid_spec=grid_spec,
        out_shape=[jax.ShapeDtypeStruct((part_rows, feat_width), out_dtype) for _ in range(cores)],
        compiler_params=pltpu.CompilerParams(
            dimension_semantics=("arbitrary",), vmem_limit_bytes=48 * 1024 * 1024
        ),
    )(row_ids, col_ids, occupied.reshape(1), core_index.reshape(1).astype(jnp.int32), tile_block, source)


def reduce_blocks(partial_value, axis, devices):
    pieces = partial_value.reshape(devices, -1, partial_value.shape[1])
    received = lax.all_to_all(pieces, axis, 0, 0, tiled=False)
    return received.astype(jnp.float32).sum(0)


def butterfly_sum(value, axes):
    for axis in axes:
        size = lax.axis_size(axis)
        step = 1
        while step < size:
            pairs = [(i, i ^ step) for i in range(size)]
            value = value + lax.ppermute(value, axis, pairs)
            step *= 2
    return value


def split_sum(value, outer, inner):
    plan = []
    for axis in outer:
        step = 1
        while step < lax.axis_size(axis):
            plan.append((axis, step))
            step *= 2
    for axis, step in plan:
        size = lax.axis_size(axis)
        low = (lax.axis_index(axis) // step) % 2 == 0
        half = value.shape[0] // 2
        head, tail = value[:half], value[half:]
        send = jnp.where(low, tail, head)
        keep = jnp.where(low, head, tail)
        value = keep + lax.ppermute(send, axis, [(i, i ^ step) for i in range(size)])
    value = butterfly_sum(value, inner)
    for axis, step in reversed(plan):
        size = lax.axis_size(axis)
        low = (lax.axis_index(axis) // step) % 2 == 0
        other = lax.ppermute(value, axis, [(i, i ^ step) for i in range(size)])
        value = jnp.concatenate(
            [jnp.where(low, value, other), jnp.where(low, other, value)], axis=0
        )
    return value


def gather_pairs(value, axis):
    size = lax.axis_size(axis)
    me = lax.axis_index(axis)
    step = size // 2
    while step >= 1:
        other = lax.ppermute(value, axis, [(i, i ^ step) for i in range(size)])
        first = (me // step) % 2 == 0
        value = jnp.concatenate(
            [jnp.where(first, value, other), jnp.where(first, other, value)], axis=0
        )
        step //= 2
    return value


def reduce_pairs_then_blocks(keep, send, outer, inner):
    outer_size = lax.axis_size(outer)
    inner_size = lax.axis_size(inner)
    keep = keep.reshape(outer_size, -1, keep.shape[1])
    send = send.reshape(outer_size, -1, send.shape[1])
    paired = keep + lax.ppermute(send, inner, [(i, inner_size - 1 - i) for i in range(inner_size)])
    received = lax.all_to_all(paired.astype(jnp.bfloat16), outer, 0, 0, tiled=False)
    return received.astype(jnp.float32).sum(0)


def silu_grad(cot_part, pre_part):
    sigma = jax.nn.sigmoid(pre_part)
    return (cot_part.astype(jnp.float32) * (sigma * (1.0 + pre_part * (1.0 - sigma)))).astype(
        jnp.bfloat16
    )


def per_device(features, weight, cotangent, tile_values, tile_rows, tile_cols, tile_count):
    node_rows = features.shape[0]
    row_devices = lax.axis_size("row")
    col_axes = ("colhi", "core")
    col_devices = lax.axis_size(col_axes)
    tile_block = tile_values[0]
    row_ids = tile_rows[0]
    col_ids = tile_cols[0]
    occupied = tile_count[0, 0]
    column_source = gather_pairs(features, "row")
    keep, send = tile_product(
        tile_block, row_ids, col_ids, occupied, column_source, col_devices * node_rows, False,
        jnp.float32, cores=lax.axis_size("core"), dev_tiles=node_rows // tile_block.shape[1],
        core_index=lax.axis_index("core"), src_bits=row_devices.bit_length() - 1,
    )
    mixed = reduce_pairs_then_blocks(keep, send, "colhi", "core")
    pre = jnp.dot(
        mixed, weight.astype(jnp.float32), precision=lax.Precision.HIGHEST,
        preferred_element_type=jnp.float32,
    )
    grad_pre = silu_grad(cotangent, pre)
    local_term = lax.dot_general(
        mixed, grad_pre.astype(jnp.float32), (((0,), (0,)), ((), ())),
        precision=lax.Precision.HIGHEST, preferred_element_type=jnp.float32,
    )
    grad_scale = float(node_rows * row_devices * col_devices) ** (-0.5)
    weight_grad = split_sum(local_term, ("row",), ("core", "colhi")) * grad_scale
    row_source = lax.all_gather(grad_pre, col_axes, axis=0, tiled=True)
    row_source, weight_grad = lax.optimization_barrier((row_source, weight_grad))
    output = jax.nn.silu(pre).astype(jnp.bfloat16)
    (back_terms,) = tile_product(
        tile_block, row_ids, col_ids, occupied, row_source, row_devices * node_rows, True,
        jnp.bfloat16,
    )
    aggregated = reduce_blocks(back_terms, "row", row_devices)
    node_grad = aggregated.astype(jnp.bfloat16)
    feature_grad = jnp.dot(node_grad, weight.T, preferred_element_type=jnp.float32).astype(
        jnp.bfloat16
    )
    return (output, feature_grad, weight_grad)


def solution(mesh):
    cores = 2
    devices = mesh.devices.reshape(mesh.shape["row"], mesh.shape["col"] // cores, cores)
    split_mesh = Mesh(devices, ("row", "colhi", "core"))
    nodes = ("row", "colhi", "core")
    blocks = ("colhi", "core")
    placed = (
        P(nodes, None),
        P(),
        P(nodes, None),
        P("row", blocks, None, None),
        P("row", blocks),
        P("row", blocks),
        P("row", blocks),
    )
    return jax.shard_map(
        per_device,
        mesh=split_mesh,
        in_specs=placed,
        out_specs=(P(nodes, None), P(nodes, None), P()),
        check_vma=False,
    )
```

```python
import jax
import jax.numpy as jnp
from jax import lax
from jax.experimental import pallas as pl
from jax.experimental.pallas import tpu as pltpu
from jax.sharding import Mesh
from jax.sharding import PartitionSpec as P

GROUP = 64


def tile_product(
    tile_block, row_ids, col_ids, occupied, source, out_rows, transpose, out_dtype,
    cores=1, dev_tiles=1, core_index=None, src_bits=0, dst_bits=0,
):
    tile_count, tile_side, _ = tile_block.shape
    feat_width = source.shape[1]
    src_rows = source.shape[0]
    row_limit = (src_rows if transpose else out_rows) // tile_side - 1
    col_limit = (out_rows if transpose else src_rows) // tile_side - 1
    steps = tile_count // GROUP
    part_rows = out_rows // cores
    if core_index is None:
        core_index = jnp.zeros((), jnp.int32)

    def kernel(rows_ref, cols_ref, cnt_ref, me_ref, tiles_ref, src_ref, *refs):
        out_refs, acc_ref = refs[:cores], refs[cores]
        g = pl.program_id(0)
        cnt = cnt_ref[0]
        me = me_ref[0]

        @pl.when(g == 0)
        def _():
            acc_ref[...] = jnp.zeros_like(acc_ref)

        @pl.when(g * GROUP < cnt)
        def _():
            for t in range(GROUP):
                k = g * GROUP + t
                r = jnp.clip(rows_ref[k], 0, row_limit)
                c = jnp.clip(cols_ref[k], 0, col_limit)
                a = tiles_ref[t]
                if transpose:
                    s = src_ref[pl.ds(pl.multiple_of(r * tile_side, tile_side), tile_side), :]
                    prod = lax.dot_general(
                        a, s, (((0,), (0,)), ((), ())), preferred_element_type=jnp.float32
                    )
                    sel = 0
                    dst_dev, dst_part = c // dev_tiles, c % dev_tiles
                    flipped = 0
                    for bit in range(dst_bits):
                        flipped = flipped + ((dst_dev // 2**bit) % 2) * 2 ** (dst_bits - 1 - bit)
                    dst = flipped * dev_tiles + dst_part if dst_bits else c
                else:
                    src_dev, src_part = c // dev_tiles, c % dev_tiles
                    flipped = 0
                    for bit in range(src_bits):
                        flipped = flipped + ((src_dev // 2**bit) % 2) * 2 ** (src_bits - 1 - bit)
                    if src_bits:
                        c = flipped * dev_tiles + src_part
                    s = src_ref[pl.ds(pl.multiple_of(c * tile_side, tile_side), tile_side), :]
                    prod = jnp.dot(a, s, preferred_element_type=jnp.float32)
                    dev, part = r // dev_tiles, r % dev_tiles
                    sel = (dev % cores - me + cores) % cores
                    dst = (dev // cores) * dev_tiles + part
                prod = jnp.where(k < cnt, prod, 0.0)
                sl = pl.ds(pl.multiple_of(dst * tile_side, tile_side), tile_side)
                acc_ref[sel, sl, :] += prod

        @pl.when(g == steps - 1)
        def _():
            for i in range(cores):
                out_refs[i][...] = acc_ref[i].astype(out_refs[i].dtype)

    def tile_map(g, rows_ref, cols_ref, cnt_ref, me_ref):
        last = jnp.maximum(cnt_ref[0] - 1, 0) // GROUP
        return (jnp.minimum(g, last), 0, 0)

    grid_spec = pltpu.PrefetchScalarGridSpec(
        num_scalar_prefetch=4,
        grid=(steps,),
        in_specs=[
            pl.BlockSpec((GROUP, tile_side, tile_side), tile_map),
            pl.BlockSpec((src_rows, feat_width), lambda g, *_: (0, 0)),
        ],
        out_specs=[
            pl.BlockSpec((part_rows, feat_width), lambda g, *_: (0, 0)) for _ in range(cores)
        ],
        scratch_shapes=[pltpu.VMEM((cores, part_rows, feat_width), jnp.float32)],
    )
    return pl.pallas_call(
        kernel,
        grid_spec=grid_spec,
        out_shape=[jax.ShapeDtypeStruct((part_rows, feat_width), out_dtype) for _ in range(cores)],
        compiler_params=pltpu.CompilerParams(
            dimension_semantics=("arbitrary",), vmem_limit_bytes=48 * 1024 * 1024
        ),
    )(row_ids, col_ids, occupied.reshape(1), core_index.reshape(1).astype(jnp.int32), tile_block, source)


def reduce_blocks(partial_value, axis, devices):
    pieces = partial_value.reshape(devices, -1, partial_value.shape[1])
    received = lax.all_to_all(pieces, axis, 0, 0, tiled=False)
    return received.astype(jnp.float32).sum(0)


def butterfly_sum(value, axes):
    for axis in axes:
        size = lax.axis_size(axis)
        step = 1
        while step < size:
            pairs = [(i, i ^ step) for i in range(size)]
            value = value + lax.ppermute(value, axis, pairs)
            step *= 2
    return value


def split_sum(value, outer, inner):
    plan = []
    for axis in outer:
        step = 1
        while step < lax.axis_size(axis):
            plan.append((axis, step))
            step *= 2
    for axis, step in plan:
        size = lax.axis_size(axis)
        low = (lax.axis_index(axis) // step) % 2 == 0
        half = value.shape[0] // 2
        head, tail = value[:half], value[half:]
        send = jnp.where(low, tail, head)
        keep = jnp.where(low, head, tail)
        value = keep + lax.ppermute(send, axis, [(i, i ^ step) for i in range(size)])
    value = butterfly_sum(value, inner)
    for axis, step in reversed(plan):
        size = lax.axis_size(axis)
        low = (lax.axis_index(axis) // step) % 2 == 0
        other = lax.ppermute(value, axis, [(i, i ^ step) for i in range(size)])
        value = jnp.concatenate(
            [jnp.where(low, value, other), jnp.where(low, other, value)], axis=0
        )
    return value


def halving_sum(value, axis):
    size = lax.axis_size(axis)
    me = lax.axis_index(axis)
    step = 1
    while step < size:
        low = (me // step) % 2 == 0
        half = value.shape[0] // 2
        head, tail = value[:half], value[half:]
        send = jnp.where(low, tail, head)
        keep = jnp.where(low, head, tail)
        value = keep + lax.ppermute(send, axis, [(i, i ^ step) for i in range(size)])
        step *= 2
    return value


def gather_pairs(value, axis):
    size = lax.axis_size(axis)
    me = lax.axis_index(axis)
    step = size // 2
    while step >= 1:
        other = lax.ppermute(value, axis, [(i, i ^ step) for i in range(size)])
        first = (me // step) % 2 == 0
        value = jnp.concatenate(
            [jnp.where(first, value, other), jnp.where(first, other, value)], axis=0
        )
        step //= 2
    return value


def reduce_pairs_then_blocks(keep, send, outer, inner):
    outer_size = lax.axis_size(outer)
    inner_size = lax.axis_size(inner)
    keep = keep.reshape(outer_size, -1, keep.shape[1])
    send = send.reshape(outer_size, -1, send.shape[1])
    paired = keep + lax.ppermute(send, inner, [(i, inner_size - 1 - i) for i in range(inner_size)])
    received = lax.all_to_all(paired.astype(jnp.bfloat16), outer, 0, 0, tiled=False)
    return received.astype(jnp.float32).sum(0)


def silu_grad(cot_part, pre_part):
    sigma = jax.nn.sigmoid(pre_part)
    return (cot_part.astype(jnp.float32) * (sigma * (1.0 + pre_part * (1.0 - sigma)))).astype(
        jnp.bfloat16
    )


def per_device(features, weight, cotangent, tile_values, tile_rows, tile_cols, tile_count):
    node_rows = features.shape[0]
    row_devices = lax.axis_size("row")
    col_axes = ("colhi", "core")
    col_devices = lax.axis_size(col_axes)
    tile_block = tile_values[0]
    row_ids = tile_rows[0]
    col_ids = tile_cols[0]
    occupied = tile_count[0, 0]
    column_source = gather_pairs(features, "row")
    keep, send = tile_product(
        tile_block, row_ids, col_ids, occupied, column_source, col_devices * node_rows, False,
        jnp.float32, cores=lax.axis_size("core"), dev_tiles=node_rows // tile_block.shape[1],
        core_index=lax.axis_index("core"), src_bits=row_devices.bit_length() - 1,
    )
    mixed = reduce_pairs_then_blocks(keep, send, "colhi", "core")
    pre = jnp.dot(
        mixed, weight.astype(jnp.float32), precision=lax.Precision.HIGHEST,
        preferred_element_type=jnp.float32,
    )
    grad_pre = silu_grad(cotangent, pre)
    local_term = lax.dot_general(
        mixed, grad_pre.astype(jnp.float32), (((0,), (0,)), ((), ())),
        precision=lax.Precision.HIGHEST, preferred_element_type=jnp.float32,
    )
    grad_scale = float(node_rows * row_devices * col_devices) ** (-0.5)
    weight_grad = split_sum(local_term, ("row",), ("core", "colhi")) * grad_scale
    row_source = lax.all_gather(grad_pre, col_axes, axis=0, tiled=True)
    row_source, weight_grad = lax.optimization_barrier((row_source, weight_grad))
    output = jax.nn.silu(pre).astype(jnp.bfloat16)
    (back_terms,) = tile_product(
        tile_block, row_ids, col_ids, occupied, row_source, row_devices * node_rows, True,
        jnp.float32, dev_tiles=node_rows // tile_block.shape[1],
        dst_bits=row_devices.bit_length() - 1,
    )
    aggregated = halving_sum(back_terms, "row")
    node_grad = aggregated.astype(jnp.bfloat16)
    feature_grad = jnp.dot(node_grad, weight.T, preferred_element_type=jnp.float32).astype(
        jnp.bfloat16
    )
    return (output, feature_grad, weight_grad)


def solution(mesh):
    cores = 2
    devices = mesh.devices.reshape(mesh.shape["row"], mesh.shape["col"] // cores, cores)
    split_mesh = Mesh(devices, ("row", "colhi", "core"))
    nodes = ("row", "colhi", "core")
    blocks = ("colhi", "core")
    placed = (
        P(nodes, None),
        P(),
        P(nodes, None),
        P("row", blocks, None, None),
        P("row", blocks),
        P("row", blocks),
        P("row", blocks),
    )
    return jax.shard_map(
        per_device,
        mesh=split_mesh,
        in_specs=placed,
        out_specs=(P(nodes, None), P(nodes, None), P()),
        check_vma=False,
    )
```
